128 devices in a mesh: term: 4 (over x_hi, core), sec: 32 (over x_lo, z, y).
Axes of the slice: x: 4 (x_hi: 2, x_lo: 2; x = x_hi * 2 + x_lo), y: 4, z: 4, core: 2. Of those that a mesh axis runs over, the one named last changes fastest.
Arguments:
- psi_tiles: bfloat16 [768, 512, 512], P('sec'), may hold values from -6 to 6
- sectors: int32 [768, 2], P('sec'), may hold values from 0 to 15
- sources: int32 [4, 768], P('term', 'sec'), may hold values from 0 to 767, as said below
- left_env: bfloat16 [4, 16, 512, 512], P('term', None, 'sec'), may hold values from -0.25 to 0.25
- right_env: bfloat16 [4, 16, 512, 512], P('term', None, 'sec'), may hold values from -0.25 to 0.25
Outputs:
- applied: bfloat16 [768, 512, 512], P('sec', 'term')
The draws below stay inside these ranges and needn't reach their ends.
Inputs may be any that keep to these rules, and one draw needn't show every extreme that they name: sources[t, k] lies in the same aligned block of 24 tiles as k, and each row maps each such block one to one onto itself.
All inputs are finite; a program needn't handle non-finite values.
Results may differ from the reference program's by a relative error of at most 0.013.
Values may be sent and summed in bfloat16 or wider, within the bound.
No kernel may reach another device: no remote copies, remote signals or barrier semaphores. Data moves between devices by JAX's collectives and lax.ppermute only.
A program may use at most 192 MiB of HBM per device.

```python
import jax
import jax.numpy as jnp

BLK = 512
NSEC = 16
TPD = 24
TILES = 768
TERMS = 4


def draw_sources(key, part):
    blocks = TILES // TPD
    keys = jax.random.split(key, TERMS * blocks)
    perms = jax.vmap(lambda one_key: jax.random.permutation(one_key, TPD))(keys)
    perms = perms.reshape(TERMS, blocks, TPD).astype(jnp.int32)
    offsets = (jnp.arange(blocks, dtype=jnp.int32) * TPD)[None, :, None]
    return (perms + offsets).reshape(TERMS, TILES).astype(jnp.int32)


def with_ends(entries, key, low, largest):
    spot = [jax.random.randint(jax.random.fold_in(key, axis), (), 0, length) for axis, length in enumerate(entries.shape)]
    widest = entries.shape.index(max(entries.shape))
    next_to = spot[:widest] + [(spot[widest] + 1) % entries.shape[widest]] + spot[widest + 1:]
    return entries.at[tuple(spot)].set(low).at[tuple(next_to)].set(largest)


def levels(key, extent, pieces, smallest, high):
    level, own = 1.0, jax.random.fold_in(key, 6)
    for axis_at, parts in pieces:
        draws = jnp.exp(jax.random.uniform(jax.random.fold_in(own, axis_at), (parts,), jnp.float32, smallest / len(pieces), high / len(pieces)))
        level = level * jnp.repeat(draws, extent[axis_at] // parts).reshape([-1 if axis == axis_at else 1 for axis in range(len(extent))])
    return level


def gaussian(key, shape, width, reach, cuts=(), kind=jnp.bfloat16):
    array = jax.random.normal(key, shape, jnp.float32) * width
    if len(cuts) > 0:
        array = levels(key, shape, cuts, -0.22, 0.18) * array
    return jnp.clip(array, min=-reach, max=reach).astype(kind)


def setup_inputs(seed: int = 0) -> dict:
    arg_keys = jax.random.split(jax.random.key(seed), 6)
    psi_tiles = gaussian(arg_keys[0], (TILES, BLK, BLK), 1.0, 6.0, ((0, 32),))
    sectors = with_ends(jax.random.randint(arg_keys[1], (TILES, 2), 0, NSEC), jax.random.fold_in(arg_keys[1], 1), 0, NSEC - 1).astype(jnp.int32)
    sources = draw_sources(jax.random.fold_in(arg_keys[5], 71), 0)
    left_env = gaussian(arg_keys[3], (TERMS, NSEC, BLK, BLK), BLK ** -0.5, 0.25, ((0, 4), (2, 32)))
    right_env = gaussian(arg_keys[4], (TERMS, NSEC, BLK, BLK), BLK ** -0.5, 0.25, ((0, 4), (2, 32)))
    return dict(psi_tiles=psi_tiles, sectors=sectors, sources=sources, left_env=left_env, right_env=right_env)


def reference(psi_tiles, sectors, sources, left_env, right_env):
    total = jnp.zeros((TILES, BLK, BLK), jnp.float32)
    for term in range(TERMS):
        moved = psi_tiles[sources[term]]
        right_sel = right_env[term][sectors[:, 1]]
        half = jnp.einsum("kij,kjl->kil", moved.astype(jnp.float32), right_sel.astype(jnp.float32)).astype(jnp.bfloat16)
        left_sel = left_env[term][sectors[:, 0]]
        term_out = jnp.einsum("kij,kjl->kil", left_sel.astype(jnp.float32), half.astype(jnp.float32)).astype(jnp.bfloat16)
        total = total + term_out.astype(jnp.float32)
    return total.astype(jnp.bfloat16)
```

```python
import jax
import jax.numpy as jnp
from jax import lax
from jax.sharding import Mesh, PartitionSpec as P

SEC = ("xl", "z", "y")
TERM = ("xh", "core")


def ring4(x, ax):
    fwd = [(i, (i + 1) % 4) for i in range(4)]
    bwd = [(i, (i - 1) % 4) for i in range(4)]
    from_prev = lax.ppermute(x, ax, fwd)
    from_next = lax.ppermute(x, ax, bwd)
    h = x.shape[0] // 2
    first = lax.ppermute(from_prev[:h], ax, fwd)
    second = lax.ppermute(from_next[h:], ax, bwd)
    me = lax.axis_index(ax)
    rel = [x, from_next, jnp.concatenate([first, second]), from_prev]
    buf = jnp.zeros((4,) + x.shape, x.dtype)
    for k in range(4):
        buf = lax.dynamic_update_index_in_dim(buf, rel[k], (me + k) % 4, 0)
    return buf


def gather_envs(left, right):
    env = jnp.concatenate([left, right], axis=0)
    other = lax.ppermute(env, "xl", [(0, 1), (1, 0)])
    low = lax.axis_index("xl") == 0
    pair = jnp.where(low, jnp.stack([env, other]), jnp.stack([other, env]))
    nsec = left.shape[0]
    by_y = ring4(pair[:, :nsec], "y")
    by_z = ring4(pair[:, nsec:], "z")
    by_y = ring4(by_y, "z")
    by_z = ring4(by_z, "y")
    width = left.shape[-1]
    left_all = jnp.transpose(by_y, (3, 2, 0, 1, 4, 5)).reshape(nsec, width, width)
    right_all = jnp.transpose(by_z, (3, 2, 1, 0, 4, 5)).reshape(nsec, width, width)
    return left_all, right_all


def body(psi_tiles, sectors, sources, left_env, right_env):
    tile_count = psi_tiles.shape[0]
    width = psi_tiles.shape[2]
    local_ids = sources[0] - lax.axis_index(SEC) * tile_count
    left_all, right_all = gather_envs(left_env[0], right_env[0])
    moved = jnp.take(psi_tiles, local_ids, axis=0)
    chosen = jnp.take(right_all, sectors[:, 1], axis=0)
    half = jnp.einsum("kij,kjl->kil", moved, chosen, preferred_element_type=jnp.float32).astype(jnp.bfloat16)
    chosen = jnp.take(left_all, sectors[:, 0], axis=0)
    out = jnp.einsum("kij,kjl->kil", chosen, half, preferred_element_type=jnp.float32).astype(jnp.bfloat16)
    rows = width // 4
    xh = lax.axis_index("xh")
    core = lax.axis_index("core")
    quarter = lambda hi, c: lax.dynamic_slice_in_dim(out, (2 * hi + c) * rows, rows, 1)
    mine = quarter(xh, core)
    to_sibling = jnp.stack([quarter(xh, 1 - core), quarter(1 - xh, 1 - core)])
    from_sibling = lax.ppermute(to_sibling, "core", [(0, 1), (1, 0)])
    partial = (quarter(1 - xh, core).astype(jnp.float32) + from_sibling[1].astype(jnp.float32)).astype(jnp.bfloat16)
    remote = lax.ppermute(partial, "xh", [(0, 1), (1, 0)])
    total = mine.astype(jnp.float32) + from_sibling[0].astype(jnp.float32) + remote.astype(jnp.float32)
    return total.astype(jnp.bfloat16)


def solution(mesh):
    fine = Mesh(mesh.devices.reshape(2, 2, 2, 4, 4), TERM + SEC)
    placed = (
        P(SEC, None, None),
        P(SEC, None),
        P(TERM, SEC),
        P(TERM, None, SEC, None),
        P(TERM, None, SEC, None),
    )
    return jax.shard_map(body, mesh=fine, in_specs=placed, out_specs=P(SEC, TERM, None), check_vma=False)
```

```python
import jax
import jax.numpy as jnp
from jax import lax
from jax.experimental import pallas as pl
from jax.experimental.pallas import tpu as pltpu
from jax.sharding import Mesh, PartitionSpec as P

SEC = ("xl", "z", "y")
TERM = ("xh", "core")
SWAP = [(0, 1), (1, 0)]


def ring4(x, ax, at):
    fwd = [(i, (i + 1) % 4) for i in range(4)]
    bwd = [(i, (i - 1) % 4) for i in range(4)]
    from_prev = lax.ppermute(x, ax, fwd)
    from_next = lax.ppermute(x, ax, bwd)
    h = x.shape[0] // 2
    first = lax.ppermute(from_prev[:h], ax, fwd)
    second = lax.ppermute(from_next[h:], ax, bwd)
    me = lax.axis_index(ax)
    rel = [x, from_next, jnp.concatenate([first, second]), from_prev]
    shape = x.shape[:at] + (4,) + x.shape[at:]
    buf = jnp.zeros(shape, x.dtype)
    for k in range(4):
        start = [0] * len(shape)
        start[at] = (me + k) % 4
        buf = lax.dynamic_update_slice(buf, jnp.expand_dims(rel[k], at), start)
    return buf


def plane_y(x):
    return ring4(ring4(x, "y", 0), "z", 0)


def plane_z(x):
    return ring4(ring4(x, "z", 0), "y", 1)


def first_kernel(src, s0, s1, xl, psi_own, psi_other, r_own, r_other, l_left, l_right, half_ref, out_ref):
    acc = jnp.dot(psi_own[...], r_own[...].reshape(-1, r_own.shape[-1]), preferred_element_type=jnp.float32)
    acc += jnp.dot(psi_other[...], r_other[...].reshape(-1, r_other.shape[-1]), preferred_element_type=jnp.float32)
    half = acc.astype(jnp.bfloat16)
    half_ref[...] = half
    cut = l_left.shape[-1]
    out = jnp.dot(l_left[...].reshape(-1, cut), half[:cut], preferred_element_type=jnp.float32)
    out += jnp.dot(l_right[...].reshape(-1, cut), half[cut:], preferred_element_type=jnp.float32)
    out_ref[...] = out.astype(out_ref.dtype)


def second_kernel(s0, half_ref, l_left, l_right, out_ref):
    cut = l_left.shape[-1]
    out = jnp.dot(l_left[...].reshape(-1, cut), half_ref[:cut], preferred_element_type=jnp.float32)
    out += jnp.dot(l_right[...].reshape(-1, cut), half_ref[cut:], preferred_element_type=jnp.float32)
    out_ref[...] = out.astype(out_ref.dtype)


def env_spec(shape, which):
    block = (shape[0], shape[1], None) + tuple(shape[3:])
    if which == 1:
        return pl.BlockSpec(block, lambda k, src, s0, s1, xl: (0, 0, s1[k], 0, 0))
    return pl.BlockSpec(block, lambda k, src, s0, s1, xl: (0, 0, s0[k], 0, 0))


def first_call(src, s0, s1, xl, psi, r_own, r_other, l_left, l_right):
    tiles, width, _ = psi.shape
    cut = width // 2
    grid = pltpu.PrefetchScalarGridSpec(
        num_scalar_prefetch=4,
        grid=(tiles,),
        in_specs=[
            pl.BlockSpec((None, width, cut), lambda k, src, s0, s1, xl: (src[k], 0, xl[0])),
            pl.BlockSpec((None, width, cut), lambda k, src, s0, s1, xl: (src[k], 0, 1 - xl[0])),
            env_spec(r_own.shape, 1),
            env_spec(r_other.shape, 1),
            env_spec(l_left.shape, 0),
            env_spec(l_right.shape, 0),
        ],
        out_specs=[
            pl.BlockSpec((None, width, width), lambda k, src, s0, s1, xl: (k, 0, 0)),
            pl.BlockSpec((None, cut, width), lambda k, src, s0, s1, xl: (k, 0, 0)),
        ],
    )
    flops = tiles * (2 * width**3 + 2 * cut * width * width)
    return pl.pallas_call(
        first_kernel,
        grid_spec=grid,
        out_shape=[
            jax.ShapeDtypeStruct((tiles, width, width), jnp.bfloat16),
            jax.ShapeDtypeStruct((tiles, cut, width), jnp.bfloat16),
        ],
        compiler_params=pltpu.CompilerParams(dimension_semantics=("arbitrary",)),
        cost_estimate=pl.CostEstimate(flops=flops, transcendentals=0, bytes_accessed=tiles * width * width * 2 * 4),
    )(src, s0, s1, xl, psi, psi, r_own, r_other, l_left, l_right)


def second_call(s0, half, l_left, l_right):
    tiles, width, _ = half.shape
    cut = width // 2
    block = lambda shape: pl.BlockSpec((shape[0], shape[1], None) + tuple(shape[3:]), lambda k, s0: (0, 0, s0[k], 0, 0))
    grid = pltpu.PrefetchScalarGridSpec(
        num_scalar_prefetch=1,
        grid=(tiles,),
        in_specs=[
            pl.BlockSpec((None, width, width), lambda k, s0: (k, 0, 0)),
            block(l_left.shape),
            block(l_right.shape),
        ],
        out_specs=pl.BlockSpec((None, cut, width), lambda k, s0: (k, 0, 0)),
    )
    return pl.pallas_call(
        second_kernel,
        grid_spec=grid,
        out_shape=jax.ShapeDtypeStruct((tiles, cut, width), jnp.bfloat16),
        compiler_params=pltpu.CompilerParams(dimension_semantics=("arbitrary",)),
        cost_estimate=pl.CostEstimate(flops=tiles * 2 * cut * width * width, transcendentals=0, bytes_accessed=tiles * width * width * 2 * 2),
    )(s0, half, l_left, l_right)


def body(psi_tiles, sectors, sources, left_env, right_env):
    tile_count, width, _ = psi_tiles.shape
    cut = width // 2
    xh = lax.axis_index("xh")
    core = lax.axis_index("core")
    xl = lax.axis_index("xl")
    left, right = left_env[0], right_env[0]
    r_own = plane_y(right)
    pair = lax.ppermute(jnp.stack([left, right]), "xl", SWAP)
    left_other, r_other_piece = pair[0], pair[1]
    r_other = plane_z(r_other_piece)
    own_is_early = xl != xh
    l_early = jnp.where(own_is_early, left, left_other)
    l_late = jnp.where(own_is_early, left_other, left)
    early_left = plane_y(l_early[..., :cut])
    early_right = plane_z(l_early[..., cut:])
    src = (sources[0] - lax.axis_index(SEC) * tile_count).astype(jnp.int32)
    s0 = sectors[:, 0].astype(jnp.int32)
    s1 = sectors[:, 1].astype(jnp.int32)
    half, out_rem = first_call(src, s0, s1, xl.reshape(1).astype(jnp.int32), psi_tiles, r_own, r_other, early_left, early_right)
    rows = width // 4
    mine_rem = lax.dynamic_slice_in_dim(out_rem, core * rows, rows, 1)
    to_sib = lax.dynamic_slice_in_dim(out_rem, (1 - core) * rows, rows, 1)
    from_sib = lax.ppermute(to_sib, "core", SWAP)
    partial = (mine_rem.astype(jnp.float32) + from_sib.astype(jnp.float32)).astype(jnp.bfloat16)
    remote = lax.ppermute(partial, "xh", SWAP)
    late_left = plane_y(l_late[..., :cut])
    late_right = plane_z(l_late[..., cut:])
    out_loc = second_call(s0, half, late_left, late_right)
    mine_loc = lax.dynamic_slice_in_dim(out_loc, core * rows, rows, 1)
    to_sib2 = lax.dynamic_slice_in_dim(out_loc, (1 - core) * rows, rows, 1)
    from_sib2 = lax.ppermute(to_sib2, "core", SWAP)
    total = mine_loc.astype(jnp.float32) + from_sib2.astype(jnp.float32) + remote.astype(jnp.float32)
    return total.astype(jnp.bfloat16)


def solution(mesh):
    fine = Mesh(mesh.devices.reshape(2, 2, 2, 4, 4), TERM + SEC)
    placed = (
        P(SEC, None, None),
        P(SEC, None),
        P(TERM, SEC),
        P(TERM, None, SEC, None),
        P(TERM, None, SEC, None),
    )
    return jax.shard_map(body, mesh=fine, in_specs=placed, out_specs=P(SEC, TERM, None), check_vma=False)
```

```python
import jax
import jax.numpy as jnp
from jax import lax
from jax.experimental import pallas as pl
from jax.experimental.pallas import tpu as pltpu
from jax.sharding import Mesh, PartitionSpec as P

SEC = ("xl", "z", "y")
TERM = ("xh", "core")
PLANE = ("z", "y")
SWAP = [(0, 1), (1, 0)]


def ring4(x, ax, at):
    fwd = [(i, (i + 1) % 4) for i in range(4)]
    bwd = [(i, (i - 1) % 4) for i in range(4)]
    from_prev = lax.ppermute(x, ax, fwd)
    from_next = lax.ppermute(x, ax, bwd)
    h = x.shape[0] // 2
    first = lax.ppermute(from_prev[:h], ax, fwd)
    second = lax.ppermute(from_next[h:], ax, bwd)
    me = lax.axis_index(ax)
    rel = [x, from_next, jnp.concatenate([first, second]), from_prev]
    shape = x.shape[:at] + (4,) + x.shape[at:]
    buf = jnp.zeros(shape, x.dtype)
    for k in range(4):
        start = [0] * len(shape)
        start[at] = (me + k) % 4
        buf = lax.dynamic_update_slice(buf, jnp.expand_dims(rel[k], at), start)
    return buf


def first_kernel(src, s0, s1, xl, psi, ra, rb, la, lb, half_ref, out_ref):
    p = psi[...]
    cut = la.shape[-1]
    ra_v = ra[...].reshape(-1, cut)
    rb_v = rb[...].reshape(-1, cut)
    half_a = jnp.dot(p, ra_v, preferred_element_type=jnp.float32).astype(jnp.bfloat16)
    half_b = jnp.dot(p, rb_v, preferred_element_type=jnp.float32).astype(jnp.bfloat16)
    half_ref[:, :cut] = half_a
    half_ref[:, cut:] = half_b
    la_v = la[...].reshape(-1, cut)
    lb_v = lb[...].reshape(-1, cut)
    out_a = jnp.dot(la_v, half_a[:cut], preferred_element_type=jnp.float32)
    out_a += jnp.dot(lb_v, half_a[cut:], preferred_element_type=jnp.float32)
    out_b = jnp.dot(la_v, half_b[:cut], preferred_element_type=jnp.float32)
    out_b += jnp.dot(lb_v, half_b[cut:], preferred_element_type=jnp.float32)
    out_ref[:, :cut] = out_a.astype(out_ref.dtype)
    out_ref[:, cut:] = out_b.astype(out_ref.dtype)


def second_kernel(half_ref, l_ref, out_ref):
    out_ref[...] = jnp.dot(l_ref[...], half_ref[...], preferred_element_type=jnp.float32).astype(out_ref.dtype)


def first_call(src, s0, s1, xl, psi, ring_part, sc_part):
    tiles, width, _ = psi.shape
    cut = width // 2
    zr, yr = ring_part.shape[2], ring_part.shape[3]
    grid = pltpu.PrefetchScalarGridSpec(
        num_scalar_prefetch=4,
        grid=(tiles,),
        in_specs=[
            pl.BlockSpec((None, width, width), lambda k, src, s0, s1, xl: (src[k], 0, 0)),
            pl.BlockSpec((2, None, zr, yr, ring_part.shape[4], cut), lambda k, src, s0, s1, xl: (0, s1[k], 0, 0, 0, 0)),
            pl.BlockSpec((2, None, sc_part.shape[2], cut), lambda k, src, s0, s1, xl: (0, s1[k], 0, 0)),
            pl.BlockSpec((None, None, zr, yr, ring_part.shape[4], cut), lambda k, src, s0, s1, xl: (2, s0[k], 0, 0, 0, 0)),
            pl.BlockSpec((None, None, sc_part.shape[2], cut), lambda k, src, s0, s1, xl: (2, s0[k], 0, 0)),
        ],
        out_specs=[
            pl.BlockSpec((None, width, width), lambda k, src, s0, s1, xl: (k, 0, 0)),
            pl.BlockSpec((None, cut, width), lambda k, src, s0, s1, xl: (k, 0, 0)),
        ],
    )
    flops = tiles * (2 * width**3 + 2 * cut * width * width)
    return pl.pallas_call(
        first_kernel,
        grid_spec=grid,
        out_shape=[
            jax.ShapeDtypeStruct((tiles, width, width), jnp.bfloat16),
            jax.ShapeDtypeStruct((tiles, cut, width), jnp.bfloat16),
        ],
        compiler_params=pltpu.CompilerParams(dimension_semantics=("arbitrary",)),
        cost_estimate=pl.CostEstimate(flops=flops, transcendentals=0, bytes_accessed=tiles * width * width * 2 * 4),
    )(src, s0, s1, xl, psi, ring_part, sc_part, ring_part, sc_part)


def second_call(s0, half, l_late):
    tiles, width, _ = half.shape
    cut = width // 2
    grid = pltpu.PrefetchScalarGridSpec(
        num_scalar_prefetch=1,
        grid=(tiles,),
        in_specs=[
            pl.BlockSpec((None, width, width), lambda k, s0: (k, 0, 0)),
            pl.BlockSpec((None, cut, width), lambda k, s0: (s0[k], 0, 0)),
        ],
        out_specs=pl.BlockSpec((None, cut, width), lambda k, s0: (k, 0, 0)),
    )
    return pl.pallas_call(
        lambda s0, h, l, o: second_kernel(h, l, o),
        grid_spec=grid,
        out_shape=jax.ShapeDtypeStruct((tiles, cut, width), jnp.bfloat16),
        compiler_params=pltpu.CompilerParams(dimension_semantics=("arbitrary",)),
        cost_estimate=pl.CostEstimate(flops=tiles * 2 * cut * width * width, transcendentals=0, bytes_accessed=tiles * width * width * 2 * 2),
    )(s0, half, l_late)


def step(psi_tiles, sectors, sources, left_env, right_env):
    tile_count, width, _ = psi_tiles.shape
    cut = width // 2
    xh = lax.axis_index("xh")
    core = lax.axis_index("core")
    xl = lax.axis_index("xl")
    left, right = left_env[0], right_env[0]
    pair = lax.ppermute(jnp.stack([left, right]), "xl", SWAP)
    left_other, right_other = pair[0], pair[1]
    low = xl == 0
    r0 = jnp.where(low, right, right_other)
    r1 = jnp.where(low, right_other, right)
    own_is_early = xl != xh
    l_early = jnp.where(own_is_early, left, left_other)
    l_late = jnp.where(own_is_early, left_other, left)
    early = jnp.stack([r0, r1, l_early])
    ring_part = ring4(ring4(early[..., :cut], "y", 2), "z", 2)
    sc_part = lax.all_gather(early[..., cut:], PLANE, axis=2, tiled=True)
    late = lax.all_gather(l_late, PLANE, axis=1, tiled=True)
    src = (sources[0] - lax.axis_index(SEC) * tile_count).astype(jnp.int32)
    s0 = sectors[:, 0].astype(jnp.int32)
    s1 = sectors[:, 1].astype(jnp.int32)
    half, out_rem = first_call(src, s0, s1, xl.reshape(1).astype(jnp.int32), psi_tiles, ring_part, sc_part)
    rows = width // 4
    mine_rem = lax.dynamic_slice_in_dim(out_rem, core * rows, rows, 1)
    to_sib = lax.dynamic_slice_in_dim(out_rem, (1 - core) * rows, rows, 1)
    from_sib = lax.ppermute(to_sib, "core", SWAP)
    partial = (mine_rem.astype(jnp.float32) + from_sib.astype(jnp.float32)).astype(jnp.bfloat16)
    remote = lax.ppermute(partial, "xh", SWAP)
    out_loc = second_call(s0, half, late)
    mine_loc = lax.dynamic_slice_in_dim(out_loc, core * rows, rows, 1)
    to_sib2 = lax.dynamic_slice_in_dim(out_loc, (1 - core) * rows, rows, 1)
    from_sib2 = lax.ppermute(to_sib2, "core", SWAP)
    total = mine_loc.astype(jnp.float32) + from_sib2.astype(jnp.float32) + remote.astype(jnp.float32)
    return total.astype(jnp.bfloat16)


def solution(mesh):
    fine = Mesh(mesh.devices.reshape(2, 2, 2, 4, 4), TERM + SEC)
    placed = (
        P(SEC, None, None),
        P(SEC, None),
        P(TERM, SEC),
        P(TERM, None, SEC, None),
        P(TERM, None, SEC, None),
    )
    return jax.shard_map(step, mesh=fine, in_specs=placed, out_specs=P(SEC, TERM, None), check_vma=False)
```

```python
import jax
import jax.numpy as jnp
from jax import lax
from jax.experimental import pallas as pl
from jax.experimental.pallas import tpu as pltpu
from jax.sharding import Mesh, PartitionSpec as P

SEC = ("xl", "z", "y")
TERM = ("xh", "core")
PLANE = ("z", "y")
SWAP = [(0, 1), (1, 0)]


def ring4(x, ax, at):
    fwd = [(i, (i + 1) % 4) for i in range(4)]
    bwd = [(i, (i - 1) % 4) for i in range(4)]
    from_prev = lax.ppermute(x, ax, fwd)
    from_next = lax.ppermute(x, ax, bwd)
    h = x.shape[0] // 2
    first = lax.ppermute(from_prev[:h], ax, fwd)
    second = lax.ppermute(from_next[h:], ax, bwd)
    me = lax.axis_index(ax)
    rel = [x, from_next, jnp.concatenate([first, second]), from_prev]
    shape = x.shape[:at] + (4,) + x.shape[at:]
    buf = jnp.zeros(shape, x.dtype)
    for k in range(4):
        start = [0] * len(shape)
        start[at] = (me + k) % 4
        buf = lax.dynamic_update_slice(buf, jnp.expand_dims(rel[k], at), start)
    return buf


def first_kernel(src, s0, s1, xl, psi, ra, rb, la, lb, half_ref, out_ref):
    p = psi[...]
    cut = la.shape[-1]
    ra_v = ra[...].reshape(-1, cut)
    rb_v = rb[...].reshape(-1, cut)
    half_a = jnp.dot(p, ra_v, preferred_element_type=jnp.float32).astype(jnp.bfloat16)
    half_b = jnp.dot(p, rb_v, preferred_element_type=jnp.float32).astype(jnp.bfloat16)
    half_ref[:, :cut] = half_a
    half_ref[:, cut:] = half_b
    la_v = la[...].reshape(-1, cut)
    lb_v = lb[...].reshape(-1, cut)
    out_a = jnp.dot(la_v, half_a[:cut], preferred_element_type=jnp.float32)
    out_a += jnp.dot(lb_v, half_a[cut:], preferred_element_type=jnp.float32)
    out_b = jnp.dot(la_v, half_b[:cut], preferred_element_type=jnp.float32)
    out_b += jnp.dot(lb_v, half_b[cut:], preferred_element_type=jnp.float32)
    out_ref[:, :cut] = out_a.astype(out_ref.dtype)
    out_ref[:, cut:] = out_b.astype(out_ref.dtype)


def second_kernel(half_ref, l_ref, out_ref):
    out_ref[...] = jnp.dot(l_ref[...], half_ref[...], preferred_element_type=jnp.float32).astype(out_ref.dtype)


def first_call(src, s0, s1, xl, psi, ring_part, sc_part):
    tiles, width = src.shape[0], psi.shape[1]
    cut = width // 2
    zr, yr = ring_part.shape[2], ring_part.shape[3]
    grid = pltpu.PrefetchScalarGridSpec(
        num_scalar_prefetch=4,
        grid=(tiles,),
        in_specs=[
            pl.BlockSpec((None, width, width), lambda k, src, s0, s1, xl: (src[k], 0, 0)),
            pl.BlockSpec((2, None, zr, yr, ring_part.shape[4], cut), lambda k, src, s0, s1, xl: (0, s1[k], 0, 0, 0, 0)),
            pl.BlockSpec((2, None, sc_part.shape[2], cut), lambda k, src, s0, s1, xl: (0, s1[k], 0, 0)),
            pl.BlockSpec((None, None, zr, yr, ring_part.shape[4], cut), lambda k, src, s0, s1, xl: (2, s0[k], 0, 0, 0, 0)),
            pl.BlockSpec((None, None, sc_part.shape[2], cut), lambda k, src, s0, s1, xl: (2, s0[k], 0, 0)),
        ],
        out_specs=[
            pl.BlockSpec((None, width, width), lambda k, src, s0, s1, xl: (k, 0, 0)),
            pl.BlockSpec((None, cut, width), lambda k, src, s0, s1, xl: (k, 0, 0)),
        ],
    )
    flops = tiles * (2 * width**3 + 2 * cut * width * width)
    return pl.pallas_call(
        first_kernel,
        grid_spec=grid,
        out_shape=[
            jax.ShapeDtypeStruct((tiles, width, width), jnp.bfloat16),
            jax.ShapeDtypeStruct((tiles, cut, width), jnp.bfloat16),
        ],
        compiler_params=pltpu.CompilerParams(dimension_semantics=("arbitrary",)),
        cost_estimate=pl.CostEstimate(flops=flops, transcendentals=0, bytes_accessed=tiles * width * width * 2 * 4),
    )(src, s0, s1, xl, psi, ring_part, sc_part, ring_part, sc_part)


def second_call(s0, half, l_late):
    tiles, width, _ = half.shape
    cut = width // 2
    grid = pltpu.PrefetchScalarGridSpec(
        num_scalar_prefetch=1,
        grid=(tiles,),
        in_specs=[
            pl.BlockSpec((None, width, width), lambda k, s0: (k, 0, 0)),
            pl.BlockSpec((None, cut, width), lambda k, s0: (s0[k], 0, 0)),
        ],
        out_specs=pl.BlockSpec((None, cut, width), lambda k, s0: (k, 0, 0)),
    )
    return pl.pallas_call(
        lambda s0, h, l, o: second_kernel(h, l, o),
        grid_spec=grid,
        out_shape=jax.ShapeDtypeStruct((tiles, cut, width), jnp.bfloat16),
        compiler_params=pltpu.CompilerParams(dimension_semantics=("arbitrary",)),
        cost_estimate=pl.CostEstimate(flops=tiles * 2 * cut * width * width, transcendentals=0, bytes_accessed=tiles * width * width * 2 * 2),
    )(s0, half, l_late)


def step(psi_tiles, sectors, sources, left_env, right_env):
    tile_count, width, _ = psi_tiles.shape
    cut = width // 2
    xh = lax.axis_index("xh")
    core = lax.axis_index("core")
    xl = lax.axis_index("xl")
    left, right = left_env[0], right_env[0]
    pair = lax.ppermute(jnp.stack([left, right]), "xl", SWAP)
    left_other, right_other = pair[0], pair[1]
    low = xl == 0
    r0 = jnp.where(low, right, right_other)
    r1 = jnp.where(low, right_other, right)
    own_is_early = xl != xh
    l_early = jnp.where(own_is_early, left, left_other)
    l_late = jnp.where(own_is_early, left_other, left)
    early = jnp.stack([r0, r1, l_early])
    ring_part = ring4(ring4(early[..., :cut], "y", 2), "z", 2)
    sc_part = lax.all_gather(early[..., cut:], PLANE, axis=2, tiled=True)
    late = lax.all_gather(l_late, PLANE, axis=1, tiled=True)
    src = (sources[0] - lax.axis_index(SEC) * tile_count).astype(jnp.int32)
    s0 = sectors[:, 0].astype(jnp.int32)
    s1 = sectors[:, 1].astype(jnp.int32)
    rows = width // 4
    chunks = 2
    per = tile_count // chunks
    xl_arg = xl.reshape(1).astype(jnp.int32)
    results = []
    pending = []
    for part in range(chunks):
        span = slice(part * per, (part + 1) * per)
        half, out_rem = first_call(src[span], s0[span], s1[span], xl_arg, psi_tiles, ring_part, sc_part)
        mine_rem = lax.dynamic_slice_in_dim(out_rem, core * rows, rows, 1)
        to_sib = lax.dynamic_slice_in_dim(out_rem, (1 - core) * rows, rows, 1)
        from_sib = lax.ppermute(to_sib, "core", SWAP)
        partial = (mine_rem.astype(jnp.float32) + from_sib.astype(jnp.float32)).astype(jnp.bfloat16)
        remote = lax.ppermute(partial, "xh", SWAP)
        pending.append((span, half, remote))
    for span, half, remote in pending:
        out_loc = second_call(s0[span], half, late)
        mine_loc = lax.dynamic_slice_in_dim(out_loc, core * rows, rows, 1)
        to_sib2 = lax.dynamic_slice_in_dim(out_loc, (1 - core) * rows, rows, 1)
        from_sib2 = lax.ppermute(to_sib2, "core", SWAP)
        total = mine_loc.astype(jnp.float32) + from_sib2.astype(jnp.float32) + remote.astype(jnp.float32)
        results.append(total.astype(jnp.bfloat16))
    return jnp.concatenate(results, axis=0)


def solution(mesh):
    fine = Mesh(mesh.devices.reshape(2, 2, 2, 4, 4), TERM + SEC)
    placed = (
        P(SEC, None, None),
        P(SEC, None),
        P(TERM, SEC),
        P(TERM, None, SEC, None),
        P(TERM, None, SEC, None),
    )
    return jax.shard_map(step, mesh=fine, in_specs=placed, out_specs=P(SEC, TERM, None), check_vma=False)
```

```python
import jax
import jax.numpy as jnp
from jax import lax
from jax.experimental import pallas as pl
from jax.experimental.pallas import tpu as pltpu
from jax.sharding import Mesh, PartitionSpec as P

SEC = ("xl", "z", "y")
TERM = ("xh", "core")
PLANE = ("z", "y")
SWAP = [(0, 1), (1, 0)]


def ring4(x, ax, at):
    fwd = [(i, (i + 1) % 4) for i in range(4)]
    bwd = [(i, (i - 1) % 4) for i in range(4)]
    from_prev = lax.ppermute(x, ax, fwd)
    from_next = lax.ppermute(x, ax, bwd)
    h = x.shape[0] // 2
    first = lax.ppermute(from_prev[:h], ax, fwd)
    second = lax.ppermute(from_next[h:], ax, bwd)
    me = lax.axis_index(ax)
    rel = [x, from_next, jnp.concatenate([first, second]), from_prev]
    shape = x.shape[:at] + (4,) + x.shape[at:]
    buf = jnp.zeros(shape, x.dtype)
    for k in range(4):
        start = [0] * len(shape)
        start[at] = (me + k) % 4
        buf = lax.dynamic_update_slice(buf, jnp.expand_dims(rel[k], at), start)
    return buf


def first_kernel(src, s0, s1, xl, psi, ra, rb, la, lb, half_ref, out_ref):
    p = psi[...]
    cut = la.shape[-1]
    ra_v = ra[...].reshape(-1, cut)
    rb_v = rb[...].reshape(-1, cut)
    half_a = jnp.dot(p, ra_v, preferred_element_type=jnp.float32).astype(jnp.bfloat16)
    half_b = jnp.dot(p, rb_v, preferred_element_type=jnp.float32).astype(jnp.bfloat16)
    half_ref[:, :cut] = half_a
    half_ref[:, cut:] = half_b
    la_v = la[...].reshape(-1, cut)
    lb_v = lb[...].reshape(-1, cut)
    out_a = jnp.dot(la_v, half_a[:cut], preferred_element_type=jnp.float32)
    out_a += jnp.dot(lb_v, half_a[cut:], preferred_element_type=jnp.float32)
    out_b = jnp.dot(la_v, half_b[:cut], preferred_element_type=jnp.float32)
    out_b += jnp.dot(lb_v, half_b[cut:], preferred_element_type=jnp.float32)
    out_ref[:, :cut] = out_a.astype(out_ref.dtype)
    out_ref[:, cut:] = out_b.astype(out_ref.dtype)


def second_kernel(half_ref, l_ref, out_ref):
    out_ref[...] = jnp.dot(l_ref[...], half_ref[...], preferred_element_type=jnp.float32).astype(out_ref.dtype)


def first_call(src, s0, s1, xl, psi, ring_part, sc_part):
    tiles, width = src.shape[0], psi.shape[1]
    cut = width // 2
    zr, yr = ring_part.shape[2], ring_part.shape[3]
    grid = pltpu.PrefetchScalarGridSpec(
        num_scalar_prefetch=4,
        grid=(tiles,),
        in_specs=[
            pl.BlockSpec((None, width, width), lambda k, src, s0, s1, xl: (src[k], 0, 0)),
            pl.BlockSpec((2, None, zr, yr, ring_part.shape[4], cut), lambda k, src, s0, s1, xl: (0, s1[k], 0, 0, 0, 0)),
            pl.BlockSpec((2, None, zr, yr, ring_part.shape[4], cut), lambda k, src, s0, s1, xl: (0, s1[k], 0, 0, 0, 0)),
            pl.BlockSpec((None, None, zr, yr, ring_part.shape[4], cut), lambda k, src, s0, s1, xl: (2, s0[k], 0, 0, 0, 0)),
            pl.BlockSpec((None, None, zr, yr, ring_part.shape[4], cut), lambda k, src, s0, s1, xl: (2, s0[k], 0, 0, 0, 0)),
        ],
        out_specs=[
            pl.BlockSpec((None, width, width), lambda k, src, s0, s1, xl: (k, 0, 0)),
            pl.BlockSpec((None, cut, width), lambda k, src, s0, s1, xl: (k, 0, 0)),
        ],
    )
    flops = tiles * (2 * width**3 + 2 * cut * width * width)
    return pl.pallas_call(
        first_kernel,
        grid_spec=grid,
        out_shape=[
            jax.ShapeDtypeStruct((tiles, width, width), jnp.bfloat16),
            jax.ShapeDtypeStruct((tiles, cut, width), jnp.bfloat16),
        ],
        compiler_params=pltpu.CompilerParams(dimension_semantics=("arbitrary",)),
        cost_estimate=pl.CostEstimate(flops=flops, transcendentals=0, bytes_accessed=tiles * width * width * 2 * 4),
    )(src, s0, s1, xl, psi, ring_part, sc_part, ring_part, sc_part)


def second_call(s0, half, l_late):
    tiles, width, _ = half.shape
    cut = width // 2
    grid = pltpu.PrefetchScalarGridSpec(
        num_scalar_prefetch=1,
        grid=(tiles,),
        in_specs=[
            pl.BlockSpec((None, width, width), lambda k, s0: (k, 0, 0)),
            pl.BlockSpec((None, cut, width), lambda k, s0: (s0[k], 0, 0)),
        ],
        out_specs=pl.BlockSpec((None, cut, width), lambda k, s0: (k, 0, 0)),
    )
    return pl.pallas_call(
        lambda s0, h, l, o: second_kernel(h, l, o),
        grid_spec=grid,
        out_shape=jax.ShapeDtypeStruct((tiles, cut, width), jnp.bfloat16),
        compiler_params=pltpu.CompilerParams(dimension_semantics=("arbitrary",)),
        cost_estimate=pl.CostEstimate(flops=tiles * 2 * cut * width * width, transcendentals=0, bytes_accessed=tiles * width * width * 2 * 2),
    )(s0, half, l_late)


def step(psi_tiles, sectors, sources, left_env, right_env):
    tile_count, width, _ = psi_tiles.shape
    cut = width // 2
    xh = lax.axis_index("xh")
    core = lax.axis_index("core")
    xl = lax.axis_index("xl")
    left, right = left_env[0], right_env[0]
    pair = lax.ppermute(jnp.stack([left, right]), "xl", SWAP)
    left_other, right_other = pair[0], pair[1]
    low = xl == 0
    r0 = jnp.where(low, right, right_other)
    r1 = jnp.where(low, right_other, right)
    own_is_early = xl != xh
    l_early = jnp.where(own_is_early, left, left_other)
    l_late = jnp.where(own_is_early, left_other, left)
    early = jnp.stack([r0, r1, l_early])
    ring_part = ring4(ring4(early[..., :cut], "y", 2), "z", 2)
    sc_part = ring4(ring4(early[..., cut:], "z", 2), "y", 3)
    late = lax.all_gather(l_late, PLANE, axis=1, tiled=True)
    src = (sources[0] - lax.axis_index(SEC) * tile_count).astype(jnp.int32)
    s0 = sectors[:, 0].astype(jnp.int32)
    s1 = sectors[:, 1].astype(jnp.int32)
    rows = width // 4
    chunks = 2
    per = tile_count // chunks
    xl_arg = xl.reshape(1).astype(jnp.int32)
    results = []
    pending = []
    for part in range(chunks):
        span = slice(part * per, (part + 1) * per)
        half, out_rem = first_call(src[span], s0[span], s1[span], xl_arg, psi_tiles, ring_part, sc_part)
        mine_rem = lax.dynamic_slice_in_dim(out_rem, core * rows, rows, 1)
        to_sib = lax.dynamic_slice_in_dim(out_rem, (1 - core) * rows, rows, 1)
        from_sib = lax.ppermute(to_sib, "core", SWAP)
        partial = (mine_rem.astype(jnp.float32) + from_sib.astype(jnp.float32)).astype(jnp.bfloat16)
        remote = lax.ppermute(partial, "xh", SWAP)
        pending.append((span, half, remote))
    for span, half, remote in pending:
        out_loc = second_call(s0[span], half, late)
        mine_loc = lax.dynamic_slice_in_dim(out_loc, core * rows, rows, 1)
        to_sib2 = lax.dynamic_slice_in_dim(out_loc, (1 - core) * rows, rows, 1)
        from_sib2 = lax.ppermute(to_sib2, "core", SWAP)
        total = mine_loc.astype(jnp.float32) + from_sib2.astype(jnp.float32) + remote.astype(jnp.float32)
        results.append(total.astype(jnp.bfloat16))
    return jnp.concatenate(results, axis=0)


def solution(mesh):
    fine = Mesh(mesh.devices.reshape(2, 2, 2, 4, 4), TERM + SEC)
    placed = (
        P(SEC, None, None),
        P(SEC, None),
        P(TERM, SEC),
        P(TERM, None, SEC, None),
        P(TERM, None, SEC, None),
    )
    return jax.shard_map(step, mesh=fine, in_specs=placed, out_specs=P(SEC, TERM, None), check_vma=False)
```
